256 devices in a mesh: shot: 32 (over x, y, z_lo), sp: 8 (over z_hi, core).
Axes of the slice: x: 4, y: 4, z: 8 (z_hi: 4, z_lo: 2; z = z_hi * 2 + z_lo), core: 2. Of those that a mesh axis runs over, the one named last changes fastest.
Arguments:
- shot_data: bfloat16 [2, 8, 12288, 4096], P(None, None, 'shot', 'sp'), may hold values from -6 to 6
- live_masks: int32 [12288, 4096], P('shot', 'sp'), may hold values 0 or 1
- spectra: bfloat16 [128, 2, 8, 1024, 256], P('shot', None, None, 'sp'), may hold values from -0.09375 to 0.09375
- plan: int32 [4, 8], replicated, may hold values from 0 to 31, as said below
Outputs:
- multiples: bfloat16 [12288, 2, 8, 256], P(('shot', 'sp'))
The draws below stay inside these ranges and needn't reach their ends.
Inputs may be any that keep to these rules, and one draw needn't show every extreme that they name: `plan`: all 4 x 8 owners are distinct shot indices; 0 and the last index both occur.
All inputs are finite; a program needn't handle non-finite values. No bound on the sum of `live_masks` on one device may be relied on, other than what follows from the above.
Results may differ from the reference program's by a relative error of at most 0.001.
Values may be sent and summed in bfloat16 or wider, within the bound.
No kernel may reach another device: no remote copies, remote signals or barrier semaphores. Data moves between devices by JAX's collectives and lax.ppermute only.
A program may use at most 128 MiB of HBM per device.

```python
import jax
import jax.numpy as jnp
from jax import lax

FREQ = 8
KB = 128
RECV = 256
STEPS = 4
OWNERS = 32
SHOTS = 12288
KTOT = 4096
SLOTS = 128
N_SP = 8


def draw_plan(key, part):
    count = STEPS * N_SP
    middle = jax.random.permutation(jax.random.fold_in(key, 11), jnp.arange(1, OWNERS - 1, dtype=jnp.int32))
    values = jnp.concatenate([jnp.array([0, OWNERS - 1], dtype=jnp.int32), middle[:count - 2]])
    values = jax.random.permutation(jax.random.fold_in(key, 12), values)
    return values.reshape(STEPS, N_SP).astype(jnp.int32)


def set_ends(values, stream_key, smallest, top_value):
    index_at = [jax.random.randint(jax.random.fold_in(stream_key, axis), (), 0, length) for axis, length in enumerate(values.shape)]
    main_axis = values.shape.index(max(values.shape))
    beside = index_at[:main_axis] + [(index_at[main_axis] + 1) % values.shape[main_axis]] + index_at[main_axis + 1:]
    return values.at[tuple(index_at)].set(smallest).at[tuple(beside)].set(top_value)


def block_levels(own_key, extent, shards, smallest, largest):
    gain = 1.0
    for axis_at, shards_of in shards:
        heights = jax.random.uniform(jax.random.fold_in(jax.random.fold_in(own_key, 6), axis_at), (shards_of,), jnp.float32, smallest / len(shards), largest / len(shards))
        gain = gain * jnp.repeat(jnp.exp(heights), extent[axis_at] // shards_of).reshape((-1,) + (1,) * (len(extent) - 1 - axis_at))
    return gain


def bell_draw(rng, shape, width, bound, split=(), held_as=jnp.bfloat16):
    entries = jax.random.normal(rng, shape, jnp.float32) * width
    if len(split) > 0:
        entries = block_levels(rng, shape, split, -0.22, 0.18) * entries
    return jnp.clip(entries, min=-bound, max=bound).astype(held_as)


def setup_inputs(seed: int = 0) -> dict:
    seeds = jax.random.split(jax.random.key(seed), 5)
    shot_data = bell_draw(seeds[0], (2, FREQ, SHOTS, KTOT), 1.0, 6.0, ((2, 32), (3, 8)))
    live_masks = set_ends((jax.random.randint(seeds[1], (SHOTS, KTOT), 0, 4) < 3).astype(jnp.int32), jax.random.fold_in(seeds[1], 1), 0, 1)
    spectra = bell_draw(seeds[2], (SLOTS, 2, FREQ, N_SP * KB, RECV), KTOT ** -0.5, 0.09375, ((0, 32), (3, 8)))
    plan = draw_plan(jax.random.fold_in(seeds[4], 71), 0)
    return {"shot_data": shot_data, "live_masks": live_masks, "spectra": spectra, "plan": plan}


def reference(shot_data, live_masks, spectra, plan):
    live = shot_data * live_masks.astype(jnp.bfloat16)[None, None]
    stored = spectra.reshape(OWNERS, STEPS, 2, FREQ, N_SP, KB, RECV)
    columns = jnp.arange(N_SP, dtype=jnp.int32)
    picked = []
    for section in range(STEPS):
        picked.append(stored[plan[section], section, :, :, columns])
    chosen = jnp.stack(picked, axis=1)
    receiver = jnp.transpose(chosen, (2, 3, 0, 1, 4, 5)).reshape(2, FREQ, KTOT, RECV)

    def one_freq(pair):
        data, recv = pair
        real_part = jnp.dot(data[0], recv[0], preferred_element_type=jnp.float32) - jnp.dot(data[1], recv[1], preferred_element_type=jnp.float32)
        imag_part = jnp.dot(data[0], recv[1], preferred_element_type=jnp.float32) + jnp.dot(data[1], recv[0], preferred_element_type=jnp.float32)
        return jnp.stack([real_part, imag_part], axis=0)

    result = lax.map(one_freq, (jnp.transpose(live, (1, 0, 2, 3)), jnp.transpose(receiver, (1, 0, 2, 3))))
    return jnp.transpose(result, (2, 1, 0, 3)).astype(jnp.bfloat16)
```

```python
import jax
import jax.numpy as jnp
from jax import lax
from jax.sharding import Mesh, PartitionSpec as P

STEPS = 4
SHOT = ("x", "y", "zl")
SP = ("zh", "c")


def gather_receivers(spectra, plan):
    n_shot = lax.psum(1, SHOT)
    sp_index = lax.axis_index(SP)
    shot_index = lax.axis_index(SHOT)
    column = lax.dynamic_index_in_dim(plan, sp_index, 1, keepdims=False)
    mine = column == shot_index
    owned_step = jnp.argmax(mine)
    block = lax.dynamic_index_in_dim(spectra, owned_step, 0, keepdims=False)
    parts, freq, kb, recv = block.shape
    split = n_shot // (parts * freq)
    pieces = block.reshape(parts * freq * split, kb // split, recv)
    got = lax.all_to_all(pieces, SHOT, 0, 0, tiled=True)
    chosen = jnp.take(got, column, axis=0)
    full = lax.all_gather(chosen, SHOT, axis=0, tiled=False)
    full = full.reshape(parts, freq, split, STEPS, kb // split, recv)
    full = jnp.transpose(full, (3, 0, 1, 2, 4, 5)).reshape(STEPS, parts, freq, kb, recv)
    return full


def body(shot_data, live_masks, spectra, plan):
    width = spectra.shape[3]
    live = shot_data * live_masks.astype(shot_data.dtype)[None, None]
    recv_all = gather_receivers(spectra, plan)
    totals = None
    for section in range(STEPS):
        recv = recv_all[section]
        window = live[:, :, :, section * width : (section + 1) * width]
        real_part = jnp.einsum(
            "fsk,fkr->sfr", window[0], recv[0], preferred_element_type=jnp.float32
        ) - jnp.einsum("fsk,fkr->sfr", window[1], recv[1], preferred_element_type=jnp.float32)
        imag_part = jnp.einsum(
            "fsk,fkr->sfr", window[0], recv[1], preferred_element_type=jnp.float32
        ) + jnp.einsum("fsk,fkr->sfr", window[1], recv[0], preferred_element_type=jnp.float32)
        piece = jnp.stack([real_part, imag_part], axis=1)
        totals = piece if totals is None else totals + piece
    return lax.psum_scatter(totals, SP, scatter_dimension=0, tiled=True).astype(jnp.bfloat16)


def solution(mesh):
    n_shot = mesh.shape["shot"]
    n_sp = mesh.shape["sp"]
    devices = mesh.devices.reshape(n_shot // 8, 4, 2, n_sp // 2, 2)
    fine = Mesh(devices, ("x", "y", "zl", "zh", "c"))
    in_specs = (
        P(None, None, SHOT, SP),
        P(SHOT, SP),
        P(SHOT, None, None, SP, None),
        P(),
    )
    out_specs = P(SHOT + SP, None, None, None)
    return jax.shard_map(body, mesh=fine, in_specs=in_specs, out_specs=out_specs, check_vma=False)
```

```python
import jax
import jax.numpy as jnp
from jax import lax
from jax.sharding import Mesh, PartitionSpec as P

STEPS = 4
SHOT = ("x", "y", "zl")
SP = ("zh", "c")


def gather_receivers(spectra, plan):
    n_shot = lax.psum(1, SHOT)
    sp_index = lax.axis_index(SP)
    shot_index = lax.axis_index(SHOT)
    column = lax.dynamic_index_in_dim(plan, sp_index, 1, keepdims=False)
    mine = column == shot_index
    owned_step = jnp.argmax(mine)
    block = lax.dynamic_index_in_dim(spectra, owned_step, 0, keepdims=False)
    parts, freq, kb, recv = block.shape
    split = n_shot // (parts * freq)
    pieces = block.reshape(parts * freq * split, kb // split, recv)
    got = lax.all_to_all(pieces, SHOT, 0, 0, tiled=True)
    chosen = jnp.take(got, column, axis=0)
    full = lax.all_gather(chosen, "zl", axis=0, tiled=False)
    full = lax.all_gather(full, "x", axis=0, tiled=False)
    full = lax.all_gather(full, "y", axis=0, tiled=False)
    n_y, n_x, n_zl = full.shape[:3]
    full = full.reshape(n_y, parts, n_x // parts, n_zl, STEPS, kb // split, recv)
    full = jnp.transpose(full, (4, 1, 2, 0, 3, 5, 6)).reshape(STEPS, parts, freq, kb, recv)
    return full


def body(shot_data, live_masks, spectra, plan):
    width = spectra.shape[3]
    live = shot_data * live_masks.astype(shot_data.dtype)[None, None]
    recv_all = gather_receivers(spectra, plan)
    totals = None
    for section in range(STEPS):
        recv = recv_all[section]
        window = live[:, :, :, section * width : (section + 1) * width]
        real_part = jnp.einsum(
            "fsk,fkr->sfr", window[0], recv[0], preferred_element_type=jnp.float32
        ) - jnp.einsum("fsk,fkr->sfr", window[1], recv[1], preferred_element_type=jnp.float32)
        imag_part = jnp.einsum(
            "fsk,fkr->sfr", window[0], recv[1], preferred_element_type=jnp.float32
        ) + jnp.einsum("fsk,fkr->sfr", window[1], recv[0], preferred_element_type=jnp.float32)
        piece = jnp.stack([real_part, imag_part], axis=1)
        totals = piece if totals is None else totals + piece
    n_zh = lax.psum(1, "zh")
    n_c = lax.psum(1, "c")
    rows = totals.shape[0]
    totals = totals.reshape(n_zh, n_c, rows // (n_zh * n_c), *totals.shape[1:])
    totals = jnp.swapaxes(totals, 0, 1).reshape(rows, *totals.shape[3:])
    totals = lax.psum_scatter(totals, "c", scatter_dimension=0, tiled=True)
    totals = lax.psum_scatter(totals, "zh", scatter_dimension=0, tiled=True)
    return totals.astype(jnp.bfloat16)


def solution(mesh):
    n_shot = mesh.shape["shot"]
    n_sp = mesh.shape["sp"]
    devices = mesh.devices.reshape(n_shot // 8, 4, 2, n_sp // 2, 2)
    fine = Mesh(devices, ("x", "y", "zl", "zh", "c"))
    in_specs = (
        P(None, None, SHOT, SP),
        P(SHOT, SP),
        P(SHOT, None, None, SP, None),
        P(),
    )
    out_specs = P(SHOT + SP, None, None, None)
    return jax.shard_map(body, mesh=fine, in_specs=in_specs, out_specs=out_specs, check_vma=False)
```

```python
import jax
import jax.numpy as jnp
from jax import lax
from jax.sharding import Mesh, PartitionSpec as P

STEPS = 4
SHOT = ("x", "y", "zl")
SP = ("zh", "c")


def gather_receivers(spectra, plan):
    n_shot = lax.psum(1, SHOT)
    sp_index = lax.axis_index(SP)
    shot_index = lax.axis_index(SHOT)
    column = lax.dynamic_index_in_dim(plan, sp_index, 1, keepdims=False)
    mine = column == shot_index
    owned_step = jnp.argmax(mine)
    block = lax.dynamic_index_in_dim(spectra, owned_step, 0, keepdims=False)
    parts, freq, kb, recv = block.shape
    split = n_shot // (parts * freq)
    pieces = block.reshape(parts * freq * split, kb // split, recv)
    got = lax.all_to_all(pieces, SHOT, 0, 0, tiled=True)
    chosen = jnp.take(got, column, axis=0)
    full = lax.all_gather(chosen, "zl", axis=0, tiled=False)
    full = lax.all_gather(full, "x", axis=0, tiled=False)
    full = lax.all_gather(full, "y", axis=0, tiled=False)
    n_y, n_x, n_zl = full.shape[:3]
    full = full.reshape(n_y, parts, n_x // parts, n_zl, STEPS, kb // split, recv)
    full = jnp.transpose(full, (4, 1, 2, 0, 3, 5, 6)).reshape(STEPS, parts, freq, kb, recv)
    return full


def body(shot_data, live_masks, spectra, plan):
    live = shot_data * live_masks.astype(shot_data.dtype)[None, None]
    recv_all = gather_receivers(spectra, plan)
    steps, parts, freq, kb, recv = recv_all.shape
    stacked = jnp.transpose(recv_all, (1, 2, 0, 3, 4)).reshape(parts, freq, steps * kb, recv)
    real_in, imag_in = stacked[0], stacked[1]
    weights = jnp.stack(
        [jnp.stack([real_in, imag_in], axis=2), jnp.stack([-imag_in, real_in], axis=2)], axis=0
    ).reshape(parts, freq, steps * kb, 2 * recv)
    out = lax.dot_general(
        live, weights, (((0, 3), (0, 2)), ((1,), (1,))), preferred_element_type=jnp.float32
    )
    out = jnp.transpose(out, (1, 0, 2))
    out = lax.psum_scatter(out, SP, scatter_dimension=0, tiled=True)
    rows = out.shape[0]
    out = out.reshape(rows, freq, 2, recv).astype(jnp.bfloat16)
    return jnp.transpose(out, (0, 2, 1, 3))


def solution(mesh):
    n_shot = mesh.shape["shot"]
    n_sp = mesh.shape["sp"]
    devices = mesh.devices.reshape(n_shot // 8, 4, 2, n_sp // 2, 2)
    fine = Mesh(devices, ("x", "y", "zl", "zh", "c"))
    in_specs = (
        P(None, None, SHOT, SP),
        P(SHOT, SP),
        P(SHOT, None, None, SP, None),
        P(),
    )
    out_specs = P(SHOT + SP, None, None, None)
    return jax.shard_map(body, mesh=fine, in_specs=in_specs, out_specs=out_specs, check_vma=False)
```

```python
import jax
import jax.numpy as jnp
from jax import lax
from jax.sharding import Mesh, PartitionSpec as P

STEPS = 4
SHOT = ("x", "y", "zl")
SP = ("zh", "c")


def gather_receivers(spectra, plan):
    n_shot = lax.psum(1, SHOT)
    sp_index = lax.axis_index(SP)
    shot_index = lax.axis_index(SHOT)
    column = lax.dynamic_index_in_dim(plan, sp_index, 1, keepdims=False)
    mine = column == shot_index
    owned_step = jnp.argmax(mine)
    block = lax.dynamic_index_in_dim(spectra, owned_step, 0, keepdims=False)
    parts, freq, kb, recv = block.shape
    split = n_shot // (parts * freq)
    pieces = block.reshape(parts * freq * split, kb // split, recv)
    got = lax.all_to_all(pieces, SHOT, 0, 0, tiled=True)
    chosen = jnp.take(got, column, axis=0)
    full = lax.all_gather(chosen, "zl", axis=0, tiled=False)
    full = lax.all_gather(full, "x", axis=0, tiled=False)
    full = lax.all_gather(full, "y", axis=0, tiled=False)
    n_y, n_x, n_zl = full.shape[:3]
    full = full.reshape(n_y, parts, n_x // parts, n_zl, STEPS, kb // split, recv)

    def part_of(p):
        return jnp.transpose(full[:, p], (1, 0, 3, 2, 4, 5)).reshape(freq, STEPS * kb, recv)

    return part_of(0), part_of(1)


def body(shot_data, live_masks, spectra, plan):
    live = shot_data * live_masks.astype(shot_data.dtype)[None, None]
    real_in, imag_in = gather_receivers(spectra, plan)
    freq, _, recv = real_in.shape
    weights = jnp.stack(
        [jnp.concatenate([real_in, imag_in], axis=-1), jnp.concatenate([-imag_in, real_in], axis=-1)], axis=0
    )
    out = lax.dot_general(
        live, weights, (((0, 3), (0, 2)), ((1,), (1,))), preferred_element_type=jnp.float32
    )
    out = jnp.transpose(out, (1, 0, 2))
    out = lax.psum_scatter(out, SP, scatter_dimension=0, tiled=True)
    rows = out.shape[0]
    out = out.reshape(rows, freq, 2, recv).astype(jnp.bfloat16)
    return jnp.transpose(out, (0, 2, 1, 3))


def solution(mesh):
    n_shot = mesh.shape["shot"]
    n_sp = mesh.shape["sp"]
    devices = mesh.devices.reshape(n_shot // 8, 4, 2, n_sp // 2, 2)
    fine = Mesh(devices, ("x", "y", "zl", "zh", "c"))
    in_specs = (
        P(None, None, SHOT, SP),
        P(SHOT, SP),
        P(SHOT, None, None, SP, None),
        P(),
    )
    out_specs = P(SHOT + SP, None, None, None)
    return jax.shard_map(body, mesh=fine, in_specs=in_specs, out_specs=out_specs, check_vma=False)
```

```python
import jax
import jax.numpy as jnp
from jax import lax
from jax.sharding import Mesh, PartitionSpec as P

STEPS = 4
SHOT = ("x", "y", "zl")
SP = ("zh", "c")


def gather_receivers(spectra, plan):
    n_shot = lax.psum(1, SHOT)
    sp_index = lax.axis_index(SP)
    shot_index = lax.axis_index(SHOT)
    column = lax.dynamic_index_in_dim(plan, sp_index, 1, keepdims=False)
    mine = column == shot_index
    owned_step = jnp.argmax(mine)
    block = lax.dynamic_index_in_dim(spectra, owned_step, 0, keepdims=False)
    parts, freq, kb, recv = block.shape
    split = n_shot // (parts * freq)
    pieces = block.reshape(parts * freq * split, kb // split, recv)
    got = lax.all_to_all(pieces, SHOT, 0, 0, tiled=True)
    chosen = jnp.take(got, column, axis=0)
    full = lax.all_gather(chosen, "zl", axis=0, tiled=False)
    full = lax.all_gather(full, "x", axis=0, tiled=False)
    full = lax.all_gather(full, "y", axis=0, tiled=False)
    n_y, n_x, n_zl = full.shape[:3]
    full = full.reshape(n_y, parts, n_x // parts, n_zl, STEPS, kb // split, recv)

    def part_of(p):
        return jnp.transpose(full[:, p], (1, 0, 3, 2, 4, 5)).reshape(freq, STEPS * kb, recv)

    return part_of(0), part_of(1)


def reduce_rows(out):
    n_zh = lax.psum(1, "zh")
    n_c = lax.psum(1, "c")
    zh = lax.axis_index("zh")
    c = lax.axis_index("c")
    rows = out.shape[0]
    blk = rows // (n_zh * n_c)
    x = out.reshape(n_zh, n_c, blk, *out.shape[1:])
    send = lax.dynamic_index_in_dim(x, n_c - 1 - c, 1, keepdims=False)
    keep = lax.dynamic_index_in_dim(x, c, 1, keepdims=False)
    got = lax.ppermute(send, "c", [(i, n_c - 1 - i) for i in range(n_c)])
    partial = keep + got
    half = blk // 2
    lo, hi = partial[:, :half], partial[:, half:]
    fwd = [(i, (i + 1) % n_zh) for i in range(n_zh)]
    bwd = [(i, (i - 1) % n_zh) for i in range(n_zh)]

    def chunk(a, index):
        return lax.dynamic_index_in_dim(a, index % n_zh, 0, keepdims=False)

    acc_lo = chunk(lo, zh + 2 * n_zh - 1)
    acc_hi = chunk(hi, zh + 1)
    for step in range(n_zh - 1):
        got_lo = lax.ppermute(acc_lo, "zh", fwd)
        got_hi = lax.ppermute(acc_hi, "zh", bwd)
        acc_lo = got_lo + chunk(lo, zh + 2 * n_zh - step - 2)
        acc_hi = got_hi + chunk(hi, zh + step + 2)
    return jnp.concatenate([acc_lo, acc_hi], axis=0)


def body(shot_data, live_masks, spectra, plan):
    live = shot_data * live_masks.astype(shot_data.dtype)[None, None]
    real_in, imag_in = gather_receivers(spectra, plan)
    freq, _, recv = real_in.shape
    weights = jnp.stack(
        [jnp.concatenate([real_in, imag_in], axis=-1), jnp.concatenate([-imag_in, real_in], axis=-1)], axis=0
    )
    out = lax.dot_general(
        live, weights, (((0, 3), (0, 2)), ((1,), (1,))), preferred_element_type=jnp.float32
    )
    out = jnp.transpose(out, (1, 0, 2))
    out = reduce_rows(out)
    rows = out.shape[0]
    out = out.reshape(rows, freq, 2, recv).astype(jnp.bfloat16)
    return jnp.transpose(out, (0, 2, 1, 3))


def solution(mesh):
    n_shot = mesh.shape["shot"]
    n_sp = mesh.shape["sp"]
    devices = mesh.devices.reshape(n_shot // 8, 4, 2, n_sp // 2, 2)
    fine = Mesh(devices, ("x", "y", "zl", "zh", "c"))
    in_specs = (
        P(None, None, SHOT, SP),
        P(SHOT, SP),
        P(SHOT, None, None, SP, None),
        P(),
    )
    out_specs = P(SHOT + SP, None, None, None)
    return jax.shard_map(body, mesh=fine, in_specs=in_specs, out_specs=out_specs, check_vma=False)
```

```python
import jax
import jax.numpy as jnp
from jax import lax
from jax.sharding import Mesh, PartitionSpec as P

STEPS = 4
SHOT = ("x", "y", "zl")
SP = ("zh", "c")


def gather_receivers(spectra, plan):
    n_shot = lax.psum(1, SHOT)
    sp_index = lax.axis_index(SP)
    shot_index = lax.axis_index(SHOT)
    column = lax.dynamic_index_in_dim(plan, sp_index, 1, keepdims=False)
    mine = column == shot_index
    owned_step = jnp.argmax(mine)
    block = lax.dynamic_index_in_dim(spectra, owned_step, 0, keepdims=False)
    parts, freq, kb, recv = block.shape
    split = n_shot // (parts * freq)
    pieces = block.reshape(parts * freq * split, kb // split, recv)
    got = lax.all_to_all(pieces, SHOT, 0, 0, tiled=True)
    chosen = jnp.take(got, column, axis=0)
    full = lax.all_gather(chosen, "zl", axis=0, tiled=False)
    n_y, n_x, n_zl = lax.psum(1, "y"), lax.psum(1, "x"), full.shape[0]
    full = lax.all_gather(full, ("y", "x"), axis=0, tiled=False)
    full = full.reshape(n_y, n_x, *full.shape[1:])
    full = full.reshape(n_y, parts, n_x // parts, n_zl, STEPS, kb // split, recv)

    def part_of(p):
        return jnp.transpose(full[:, p], (1, 0, 3, 2, 4, 5)).reshape(freq, STEPS * kb, recv)

    return part_of(0), part_of(1)


def body(shot_data, live_masks, spectra, plan):
    live = shot_data * live_masks.astype(shot_data.dtype)[None, None]
    real_in, imag_in = gather_receivers(spectra, plan)
    freq, _, recv = real_in.shape
    weights = jnp.stack(
        [jnp.concatenate([real_in, imag_in], axis=-1), jnp.concatenate([-imag_in, real_in], axis=-1)], axis=0
    )
    out = lax.dot_general(
        live, weights, (((0, 3), (0, 2)), ((1,), (1,))), preferred_element_type=jnp.float32
    )
    out = jnp.transpose(out, (1, 0, 2))
    out = lax.psum_scatter(out, SP, scatter_dimension=0, tiled=True)
    rows = out.shape[0]
    out = out.reshape(rows, freq, 2, recv).astype(jnp.bfloat16)
    return jnp.transpose(out, (0, 2, 1, 3))


def solution(mesh):
    n_shot = mesh.shape["shot"]
    n_sp = mesh.shape["sp"]
    devices = mesh.devices.reshape(n_shot // 8, 4, 2, n_sp // 2, 2)
    fine = Mesh(devices, ("x", "y", "zl", "zh", "c"))
    in_specs = (
        P(None, None, SHOT, SP),
        P(SHOT, SP),
        P(SHOT, None, None, SP, None),
        P(),
    )
    out_specs = P(SHOT + SP, None, None, None)
    return jax.shard_map(body, mesh=fine, in_specs=in_specs, out_specs=out_specs, check_vma=False)
```

```python
import jax
import jax.numpy as jnp
from jax import lax
from jax.sharding import Mesh, PartitionSpec as P

STEPS = 4
SHOT = ("x", "y", "zl")
SP = ("zh", "c")


def gather_receivers(spectra, plan, group, n_groups, after=None):
    n_shot = lax.psum(1, SHOT)
    sp_index = lax.axis_index(SP)
    shot_index = lax.axis_index(SHOT)
    column = lax.dynamic_index_in_dim(plan, sp_index, 1, keepdims=False)
    owned_step = jnp.argmax(column == shot_index)
    block = lax.dynamic_index_in_dim(spectra, owned_step, 0, keepdims=False)
    parts, freq, kb, recv = block.shape
    fg = freq // n_groups
    block = block[:, group * fg : (group + 1) * fg]
    quarters = n_shot // (parts * fg)
    pieces = block.reshape(n_shot, kb // quarters, recv)
    if after is not None:
        pieces = pieces + (after[0, 0, 0] * 0).astype(pieces.dtype)
    got = lax.all_to_all(pieces, SHOT, 0, 0, tiled=True)
    chosen = jnp.take(got, column, axis=0)
    full = lax.all_gather(chosen, "zl", axis=0, tiled=False)
    n_y, n_x, n_zl = lax.psum(1, "y"), lax.psum(1, "x"), full.shape[0]
    full = lax.all_gather(full, ("y", "x"), axis=0, tiled=False)
    full = full.reshape(n_y, n_x, *full.shape[1:])
    full = full.reshape(n_y // 2, 2, parts, n_x // parts, n_zl, STEPS, kb // quarters, recv)

    def part_of(p):
        return jnp.transpose(full[:, :, p], (2, 0, 4, 1, 3, 5, 6)).reshape(fg, STEPS * kb, recv)

    return part_of(0), part_of(1)


def reduce_rows(out):
    n_zh = lax.psum(1, "zh")
    n_c = lax.psum(1, "c")
    zh = lax.axis_index("zh")
    c = lax.axis_index("c")
    rows = out.shape[0]
    blk = rows // (n_zh * n_c)
    x = out.reshape(n_zh, n_c, blk, *out.shape[1:])
    send = lax.dynamic_index_in_dim(x, n_c - 1 - c, 1, keepdims=False)
    keep = lax.dynamic_index_in_dim(x, c, 1, keepdims=False)
    got = lax.ppermute(send, "c", [(i, n_c - 1 - i) for i in range(n_c)])
    partial = keep + got
    half = blk // 2
    lo, hi = partial[:, :half], partial[:, half:]
    fwd = [(i, (i + 1) % n_zh) for i in range(n_zh)]
    bwd = [(i, (i - 1) % n_zh) for i in range(n_zh)]

    def chunk(a, index):
        return lax.dynamic_index_in_dim(a, index % n_zh, 0, keepdims=False)

    acc_lo = chunk(lo, zh + 2 * n_zh - 1)
    acc_hi = chunk(hi, zh + 1)
    for step in range(n_zh - 1):
        got_lo = lax.ppermute(acc_lo, "zh", fwd)
        got_hi = lax.ppermute(acc_hi, "zh", bwd)
        acc_lo = got_lo + chunk(lo, zh + 2 * n_zh - step - 2)
        acc_hi = got_hi + chunk(hi, zh + step + 2)
    return jnp.concatenate([acc_lo, acc_hi], axis=0)


def body(shot_data, live_masks, spectra, plan):
    mask = live_masks.astype(shot_data.dtype)[None, None]
    freq = shot_data.shape[1]
    n_groups = 2
    fg = freq // n_groups
    results = []
    prev = None
    for group in range(n_groups):
        real_in, imag_in = gather_receivers(spectra, plan, group, n_groups, prev)
        recv = real_in.shape[-1]
        weights = jnp.stack(
            [jnp.concatenate([real_in, imag_in], axis=-1), jnp.concatenate([-imag_in, real_in], axis=-1)], axis=0
        )
        if results:
            both_halves = results[-1][0, 0, 0] + results[-1][-1, 0, 0]
            weights = weights + (both_halves * 0).astype(weights.dtype)
        live = shot_data[:, group * fg : (group + 1) * fg] * mask
        out = lax.dot_general(
            live, weights, (((0, 3), (0, 2)), ((1,), (1,))), preferred_element_type=jnp.float32
        )
        out = jnp.transpose(out, (1, 0, 2))
        prev = out
        results.append(reduce_rows(out))
    out = jnp.concatenate(results, axis=1)
    rows = out.shape[0]
    out = out.reshape(rows, freq, 2, recv).astype(jnp.bfloat16)
    return jnp.transpose(out, (0, 2, 1, 3))


def solution(mesh):
    n_shot = mesh.shape["shot"]
    n_sp = mesh.shape["sp"]
    devices = mesh.devices.reshape(n_shot // 8, 4, 2, n_sp // 2, 2)
    fine = Mesh(devices, ("x", "y", "zl", "zh", "c"))
    in_specs = (
        P(None, None, SHOT, SP),
        P(SHOT, SP),
        P(SHOT, None, None, SP, None),
        P(),
    )
    out_specs = P(SHOT + SP, None, None, None)
    return jax.shard_map(body, mesh=fine, in_specs=in_specs, out_specs=out_specs, check_vma=False)
```

```python
import jax
import jax.numpy as jnp
from jax import lax
from jax.sharding import Mesh, PartitionSpec as P

STEPS = 4
SHOT = ("x", "y", "zl")
SP = ("zh", "c")


def gather_receivers(spectra, plan):
    n_shot = lax.psum(1, SHOT)
    sp_index = lax.axis_index(SP)
    shot_index = lax.axis_index(SHOT)
    column = lax.dynamic_index_in_dim(plan, sp_index, 1, keepdims=False)
    mine = column == shot_index
    owned_step = jnp.argmax(mine)
    block = lax.dynamic_index_in_dim(spectra, owned_step, 0, keepdims=False)
    parts, freq, kb, recv = block.shape
    split = n_shot // (parts * freq)
    pieces = block.reshape(parts * freq * split, kb // split, recv)
    got = lax.all_to_all(pieces, SHOT, 0, 0, tiled=True)
    chosen = jnp.take(got, column, axis=0)
    full = lax.all_gather(chosen, "zl", axis=0, tiled=False)
    n_y, n_x, n_zl = lax.psum(1, "y"), lax.psum(1, "x"), full.shape[0]
    full = lax.all_gather(full, ("y", "x"), axis=0, tiled=False)
    full = full.reshape(n_y, n_x, *full.shape[1:])
    full = full.reshape(n_y, parts, n_x // parts, n_zl, STEPS, kb // split, recv)

    def part_of(p):
        return jnp.transpose(full[:, p], (1, 0, 3, 2, 4, 5)).reshape(freq, STEPS * kb, recv)

    return part_of(0), part_of(1)


def reduce_rows(out):
    n_zh = lax.psum(1, "zh")
    n_c = lax.psum(1, "c")
    zh = lax.axis_index("zh")
    c = lax.axis_index("c")
    rows = out.shape[0]
    blk = rows // (n_zh * n_c)
    x = out.reshape(n_zh, n_c, blk, *out.shape[1:])
    send = lax.dynamic_index_in_dim(x, n_c - 1 - c, 1, keepdims=False)
    keep = lax.dynamic_index_in_dim(x, c, 1, keepdims=False)
    got = lax.ppermute(send, "c", [(i, n_c - 1 - i) for i in range(n_c)])
    partial = keep + got
    half = blk // 2
    lo, hi = partial[:, :half], partial[:, half:]
    fwd = [(i, (i + 1) % n_zh) for i in range(n_zh)]
    bwd = [(i, (i - 1) % n_zh) for i in range(n_zh)]

    def chunk(a, index):
        return lax.dynamic_index_in_dim(a, index % n_zh, 0, keepdims=False)

    acc_lo = chunk(lo, zh + 2 * n_zh - 1)
    acc_hi = chunk(hi, zh + 1)
    for step in range(n_zh - 1):
        got_lo = lax.ppermute(acc_lo, "zh", fwd)
        got_hi = lax.ppermute(acc_hi, "zh", bwd)
        acc_lo = got_lo + chunk(lo, zh + 2 * n_zh - step - 2)
        acc_hi = got_hi + chunk(hi, zh + step + 2)
    return jnp.concatenate([acc_lo, acc_hi], axis=0)


def body(shot_data, live_masks, spectra, plan):
    live = shot_data * live_masks.astype(shot_data.dtype)[None, None]
    real_in, imag_in = gather_receivers(spectra, plan)
    freq, _, recv = real_in.shape
    weights = jnp.stack(
        [jnp.concatenate([real_in, imag_in], axis=-1), jnp.concatenate([-imag_in, real_in], axis=-1)], axis=0
    )
    out = lax.dot_general(
        live, weights, (((0, 3), (0, 2)), ((1,), (1,))), preferred_element_type=jnp.float32
    )
    out = jnp.transpose(out, (1, 0, 2))
    half = out.shape[1] // 2
    by_scatter = lax.psum_scatter(out[:, :half], SP, scatter_dimension=0, tiled=True)
    by_ring = reduce_rows(out[:, half:])
    out = jnp.concatenate([by_scatter, by_ring], axis=1)
    rows = out.shape[0]
    out = out.reshape(rows, freq, 2, recv).astype(jnp.bfloat16)
    return jnp.transpose(out, (0, 2, 1, 3))


def solution(mesh):
    n_shot = mesh.shape["shot"]
    n_sp = mesh.shape["sp"]
    devices = mesh.devices.reshape(n_shot // 8, 4, 2, n_sp // 2, 2)
    fine = Mesh(devices, ("x", "y", "zl", "zh", "c"))
    in_specs = (
        P(None, None, SHOT, SP),
        P(SHOT, SP),
        P(SHOT, None, None, SP, None),
        P(),
    )
    out_specs = P(SHOT + SP, None, None, None)
    return jax.shard_map(body, mesh=fine, in_specs=in_specs, out_specs=out_specs, check_vma=False)
```

```python
import jax
import jax.numpy as jnp
from jax import lax
from jax.sharding import Mesh, PartitionSpec as P

STEPS = 4
SHOT = ("x", "y", "zl")
SP = ("zh", "c")


def ring_gather(piece, axis):
    n = lax.psum(1, axis)
    me = lax.axis_index(axis)
    fwd = [(i, (i + 1) % n) for i in range(n)]
    bwd = [(i, (i - 1) % n) for i in range(n)]
    from_left = lax.ppermute(piece, axis, fwd)
    from_right = lax.ppermute(piece, axis, bwd)
    half = piece.shape[0] // 2
    far = jnp.concatenate(
        [lax.ppermute(from_left[:half], axis, fwd), lax.ppermute(from_right[half:], axis, bwd)], axis=0
    )
    rel = jnp.stack([piece, from_right, far, from_left], axis=0)
    doubled = jnp.concatenate([rel, rel], axis=0)
    return lax.dynamic_slice_in_dim(doubled, (n - me) % n, n, axis=0)


def gather_receivers(spectra, plan):
    n_shot = lax.psum(1, SHOT)
    sp_index = lax.axis_index(SP)
    shot_index = lax.axis_index(SHOT)
    column = lax.dynamic_index_in_dim(plan, sp_index, 1, keepdims=False)
    mine = column == shot_index
    owned_step = jnp.argmax(mine)
    block = lax.dynamic_index_in_dim(spectra, owned_step, 0, keepdims=False)
    parts, freq, kb, recv = block.shape
    split = n_shot // (parts * freq)
    pieces = block.reshape(parts * freq * split, kb // split, recv)
    got = lax.all_to_all(pieces, SHOT, 0, 0, tiled=True)
    chosen = jnp.take(got, column, axis=0)
    full = lax.all_gather(chosen, "zl", axis=0, tiled=False)
    n_y, n_x, n_zl = lax.psum(1, "y"), lax.psum(1, "x"), full.shape[0]
    first = ring_gather(ring_gather(full[:, : STEPS // 2], "x"), "y")
    second = ring_gather(ring_gather(full[:, STEPS // 2 :], "y"), "x")
    full = jnp.concatenate([first, jnp.swapaxes(second, 0, 1)], axis=3)
    full = full.reshape(n_y, parts, n_x // parts, n_zl, STEPS, kb // split, recv)

    def part_of(p):
        return jnp.transpose(full[:, p], (1, 0, 3, 2, 4, 5)).reshape(freq, STEPS * kb, recv)

    return part_of(0), part_of(1)


def reduce_rows(out):
    n_zh = lax.psum(1, "zh")
    n_c = lax.psum(1, "c")
    zh = lax.axis_index("zh")
    c = lax.axis_index("c")
    rows = out.shape[0]
    blk = rows // (n_zh * n_c)
    x = out.reshape(n_zh, n_c, blk, *out.shape[1:])
    send = lax.dynamic_index_in_dim(x, n_c - 1 - c, 1, keepdims=False)
    keep = lax.dynamic_index_in_dim(x, c, 1, keepdims=False)
    got = lax.ppermute(send, "c", [(i, n_c - 1 - i) for i in range(n_c)])
    partial = keep + got
    half = blk // 2
    lo, hi = partial[:, :half], partial[:, half:]
    fwd = [(i, (i + 1) % n_zh) for i in range(n_zh)]
    bwd = [(i, (i - 1) % n_zh) for i in range(n_zh)]

    def chunk(a, index):
        return lax.dynamic_index_in_dim(a, index % n_zh, 0, keepdims=False)

    acc_lo = chunk(lo, zh + 2 * n_zh - 1)
    acc_hi = chunk(hi, zh + 1)
    for step in range(n_zh - 1):
        got_lo = lax.ppermute(acc_lo, "zh", fwd)
        got_hi = lax.ppermute(acc_hi, "zh", bwd)
        acc_lo = got_lo + chunk(lo, zh + 2 * n_zh - step - 2)
        acc_hi = got_hi + chunk(hi, zh + step + 2)
    return jnp.concatenate([acc_lo, acc_hi], axis=0)


def body(shot_data, live_masks, spectra, plan):
    live = shot_data * live_masks.astype(shot_data.dtype)[None, None]
    real_in, imag_in = gather_receivers(spectra, plan)
    freq, _, recv = real_in.shape
    weights = jnp.stack(
        [jnp.concatenate([real_in, imag_in], axis=-1), jnp.concatenate([-imag_in, real_in], axis=-1)], axis=0
    )
    out = lax.dot_general(
        live, weights, (((0, 3), (0, 2)), ((1,), (1,))), preferred_element_type=jnp.float32
    )
    out = jnp.transpose(out, (1, 0, 2))
    half = out.shape[1] // 2
    by_scatter = lax.psum_scatter(out[:, :half], SP, scatter_dimension=0, tiled=True)
    by_ring = reduce_rows(out[:, half:])
    out = jnp.concatenate([by_scatter, by_ring], axis=1)
    rows = out.shape[0]
    out = out.reshape(rows, freq, 2, recv).astype(jnp.bfloat16)
    return jnp.transpose(out, (0, 2, 1, 3))


def solution(mesh):
    n_shot = mesh.shape["shot"]
    n_sp = mesh.shape["sp"]
    devices = mesh.devices.reshape(n_shot // 8, 4, 2, n_sp // 2, 2)
    fine = Mesh(devices, ("x", "y", "zl", "zh", "c"))
    in_specs = (
        P(None, None, SHOT, SP),
        P(SHOT, SP),
        P(SHOT, None, None, SP, None),
        P(),
    )
    out_specs = P(SHOT + SP, None, None, None)
    return jax.shard_map(body, mesh=fine, in_specs=in_specs, out_specs=out_specs, check_vma=False)
```

```python
import jax
import jax.numpy as jnp
from jax import lax
from jax.sharding import Mesh, PartitionSpec as P

STEPS = 4
SHOT = ("x", "y", "zl")
SP = ("zh", "c")


def ring_gather(piece, axis):
    n = lax.psum(1, axis)
    me = lax.axis_index(axis)
    fwd = [(i, (i + 1) % n) for i in range(n)]
    bwd = [(i, (i - 1) % n) for i in range(n)]
    from_left = lax.ppermute(piece, axis, fwd)
    from_right = lax.ppermute(piece, axis, bwd)
    half = piece.shape[0] // 2
    far = jnp.concatenate(
        [lax.ppermute(from_left[:half], axis, fwd), lax.ppermute(from_right[half:], axis, bwd)], axis=0
    )
    rel = jnp.stack([piece, from_right, far, from_left], axis=0)
    doubled = jnp.concatenate([rel, rel], axis=0)
    return lax.dynamic_slice_in_dim(doubled, (n - me) % n, n, axis=0)


def gather_receivers(spectra, plan, group, n_groups, after=None):
    n_shot = lax.psum(1, SHOT)
    sp_index = lax.axis_index(SP)
    shot_index = lax.axis_index(SHOT)
    column = lax.dynamic_index_in_dim(plan, sp_index, 1, keepdims=False)
    owned_step = jnp.argmax(column == shot_index)
    block = lax.dynamic_index_in_dim(spectra, owned_step, 0, keepdims=False)
    parts, freq, kb, recv = block.shape
    fg = freq // n_groups
    block = block[:, group * fg : (group + 1) * fg]
    quarters = n_shot // (parts * fg)
    pieces = block.reshape(n_shot, kb // quarters, recv)
    if after is not None:
        pieces = pieces + (after[0, 0, 0] * 0).astype(pieces.dtype)
    got = lax.all_to_all(pieces, SHOT, 0, 0, tiled=True)
    chosen = jnp.take(got, column, axis=0)
    full = lax.all_gather(chosen, "zl", axis=0, tiled=False)
    n_y, n_x, n_zl = lax.psum(1, "y"), lax.psum(1, "x"), full.shape[0]
    first = ring_gather(ring_gather(full[:, : STEPS // 2], "x"), "y")
    second = ring_gather(ring_gather(full[:, STEPS // 2 :], "y"), "x")
    full = jnp.concatenate([first, jnp.swapaxes(second, 0, 1)], axis=3)
    full = full.reshape(n_y // 2, 2, parts, n_x // parts, n_zl, STEPS, kb // quarters, recv)

    def part_of(p):
        return jnp.transpose(full[:, :, p], (2, 0, 4, 1, 3, 5, 6)).reshape(fg, STEPS * kb, recv)

    return part_of(0), part_of(1)


def reduce_rows(out):
    n_zh = lax.psum(1, "zh")
    n_c = lax.psum(1, "c")
    zh = lax.axis_index("zh")
    c = lax.axis_index("c")
    rows = out.shape[0]
    blk = rows // (n_zh * n_c)
    x = out.reshape(n_zh, n_c, blk, *out.shape[1:])
    send = lax.dynamic_index_in_dim(x, n_c - 1 - c, 1, keepdims=False)
    keep = lax.dynamic_index_in_dim(x, c, 1, keepdims=False)
    got = lax.ppermute(send, "c", [(i, n_c - 1 - i) for i in range(n_c)])
    partial = keep + got
    half = blk // 2
    lo, hi = partial[:, :half], partial[:, half:]
    fwd = [(i, (i + 1) % n_zh) for i in range(n_zh)]
    bwd = [(i, (i - 1) % n_zh) for i in range(n_zh)]

    def chunk(a, index):
        return lax.dynamic_index_in_dim(a, index % n_zh, 0, keepdims=False)

    acc_lo = chunk(lo, zh + 2 * n_zh - 1)
    acc_hi = chunk(hi, zh + 1)
    for step in range(n_zh - 1):
        got_lo = lax.ppermute(acc_lo, "zh", fwd)
        got_hi = lax.ppermute(acc_hi, "zh", bwd)
        acc_lo = got_lo + chunk(lo, zh + 2 * n_zh - step - 2)
        acc_hi = got_hi + chunk(hi, zh + step + 2)
    return jnp.concatenate([acc_lo, acc_hi], axis=0)


def reduce_split(out):
    half = out.shape[1] // 2
    by_scatter = lax.psum_scatter(out[:, :half], SP, scatter_dimension=0, tiled=True)
    by_ring = reduce_rows(out[:, half:])
    return jnp.concatenate([by_scatter, by_ring], axis=1)


def body(shot_data, live_masks, spectra, plan):
    mask = live_masks.astype(shot_data.dtype)[None, None]
    freq = shot_data.shape[1]
    n_groups = 2
    fg = freq // n_groups
    results = []
    prev = None
    for group in range(n_groups):
        real_in, imag_in = gather_receivers(spectra, plan, group, n_groups, prev)
        recv = real_in.shape[-1]
        weights = jnp.stack(
            [jnp.concatenate([real_in, imag_in], axis=-1), jnp.concatenate([-imag_in, real_in], axis=-1)], axis=0
        )
        if results:
            both_ends = results[-1][0, 0, 0] + results[-1][0, -1, 0] + results[-1][-1, 0, 0] + results[-1][-1, -1, 0]
            weights = weights + (both_ends * 0).astype(weights.dtype)
        live = shot_data[:, group * fg : (group + 1) * fg] * mask
        out = lax.dot_general(
            live, weights, (((0, 3), (0, 2)), ((1,), (1,))), preferred_element_type=jnp.float32
        )
        out = jnp.transpose(out, (1, 0, 2))
        prev = out
        results.append(reduce_split(out))
    out = jnp.concatenate(results, axis=1)
    rows = out.shape[0]
    out = out.reshape(rows, freq, 2, recv).astype(jnp.bfloat16)
    return jnp.transpose(out, (0, 2, 1, 3))


def solution(mesh):
    n_shot = mesh.shape["shot"]
    n_sp = mesh.shape["sp"]
    devices = mesh.devices.reshape(n_shot // 8, 4, 2, n_sp // 2, 2)
    fine = Mesh(devices, ("x", "y", "zl", "zh", "c"))
    in_specs = (
        P(None, None, SHOT, SP),
        P(SHOT, SP),
        P(SHOT, None, None, SP, None),
        P(),
    )
    out_specs = P(SHOT + SP, None, None, None)
    return jax.shard_map(body, mesh=fine, in_specs=in_specs, out_specs=out_specs, check_vma=False)
```

```python
import jax
import jax.numpy as jnp
from jax import lax
from jax.sharding import Mesh, PartitionSpec as P

STEPS = 4
SHOT = ("x", "y", "zl")
SP = ("zh", "c")


def ring_gather(piece, axis):
    n = lax.psum(1, axis)
    me = lax.axis_index(axis)
    fwd = [(i, (i + 1) % n) for i in range(n)]
    bwd = [(i, (i - 1) % n) for i in range(n)]
    from_left = lax.ppermute(piece, axis, fwd)
    from_right = lax.ppermute(piece, axis, bwd)
    half = piece.shape[0] // 2
    far = jnp.concatenate(
        [lax.ppermute(from_left[:half], axis, fwd), lax.ppermute(from_right[half:], axis, bwd)], axis=0
    )
    rel = jnp.stack([piece, from_right, far, from_left], axis=0)
    doubled = jnp.concatenate([rel, rel], axis=0)
    return lax.dynamic_slice_in_dim(doubled, (n - me) % n, n, axis=0)


def gather_receivers(spectra, plan):
    n_shot = lax.psum(1, SHOT)
    sp_index = lax.axis_index(SP)
    shot_index = lax.axis_index(SHOT)
    column = lax.dynamic_index_in_dim(plan, sp_index, 1, keepdims=False)
    mine = column == shot_index
    owned_step = jnp.argmax(mine)
    block = lax.dynamic_index_in_dim(spectra, owned_step, 0, keepdims=False)
    parts, freq, kb, recv = block.shape
    split = n_shot // (parts * freq)
    pieces = block.reshape(parts * freq * split, kb // split, recv)
    got = lax.all_to_all(pieces, SHOT, 0, 0, tiled=True)
    chosen = jnp.take(got, column, axis=0)
    n_zl = lax.psum(1, "zl")
    me_zl = lax.axis_index("zl")
    other = lax.ppermute(chosen, "zl", [(i, n_zl - 1 - i) for i in range(n_zl)])
    pair = jnp.stack([chosen, other, chosen], axis=0)
    full = lax.dynamic_slice_in_dim(pair, (n_zl - me_zl) % n_zl, n_zl, axis=0)
    n_y, n_x, n_zl = lax.psum(1, "y"), lax.psum(1, "x"), full.shape[0]
    first = ring_gather(ring_gather(full[:, : STEPS // 2], "x"), "y")
    second = ring_gather(ring_gather(full[:, STEPS // 2 :], "y"), "x")
    full = jnp.concatenate([first, jnp.swapaxes(second, 0, 1)], axis=3)
    full = full.reshape(n_y, parts, n_x // parts, n_zl, STEPS, kb // split, recv)

    def part_of(p):
        return jnp.transpose(full[:, p], (1, 0, 3, 2, 4, 5)).reshape(freq, STEPS * kb, recv)

    return part_of(0), part_of(1)


def reduce_rows(out):
    n_zh = lax.psum(1, "zh")
    n_c = lax.psum(1, "c")
    zh = lax.axis_index("zh")
    c = lax.axis_index("c")
    rows = out.shape[0]
    blk = rows // (n_zh * n_c)
    x = out.reshape(n_zh, n_c, blk, *out.shape[1:])
    send = lax.dynamic_index_in_dim(x, n_c - 1 - c, 1, keepdims=False)
    keep = lax.dynamic_index_in_dim(x, c, 1, keepdims=False)
    got = lax.ppermute(send, "c", [(i, n_c - 1 - i) for i in range(n_c)])
    partial = keep + got
    half = blk // 2
    lo, hi = partial[:, :half], partial[:, half:]
    fwd = [(i, (i + 1) % n_zh) for i in range(n_zh)]
    bwd = [(i, (i - 1) % n_zh) for i in range(n_zh)]

    def chunk(a, index):
        return lax.dynamic_index_in_dim(a, index % n_zh, 0, keepdims=False)

    acc_lo = chunk(lo, zh + 2 * n_zh - 1)
    acc_hi = chunk(hi, zh + 1)
    for step in range(n_zh - 1):
        got_lo = lax.ppermute(acc_lo, "zh", fwd)
        got_hi = lax.ppermute(acc_hi, "zh", bwd)
        acc_lo = got_lo + chunk(lo, zh + 2 * n_zh - step - 2)
        acc_hi = got_hi + chunk(hi, zh + step + 2)
    return jnp.concatenate([acc_lo, acc_hi], axis=0)


def body(shot_data, live_masks, spectra, plan):
    live = shot_data * live_masks.astype(shot_data.dtype)[None, None]
    real_in, imag_in = gather_receivers(spectra, plan)
    freq, _, recv = real_in.shape
    weights = jnp.stack(
        [jnp.concatenate([real_in, imag_in], axis=-1), jnp.concatenate([-imag_in, real_in], axis=-1)], axis=0
    )
    out = lax.dot_general(
        live, weights, (((0, 3), (0, 2)), ((1,), (1,))), preferred_element_type=jnp.float32
    )
    out = jnp.transpose(out, (1, 0, 2))
    half = out.shape[1] // 2
    by_scatter = lax.psum_scatter(out[:, :half], SP, scatter_dimension=0, tiled=True)
    by_ring = reduce_rows(out[:, half:])
    out = jnp.concatenate([by_scatter, by_ring], axis=1)
    rows = out.shape[0]
    out = out.reshape(rows, freq, 2, recv).astype(jnp.bfloat16)
    return jnp.transpose(out, (0, 2, 1, 3))


def solution(mesh):
    n_shot = mesh.shape["shot"]
    n_sp = mesh.shape["sp"]
    devices = mesh.devices.reshape(n_shot // 8, 4, 2, n_sp // 2, 2)
    fine = Mesh(devices, ("x", "y", "zl", "zh", "c"))
    in_specs = (
        P(None, None, SHOT, SP),
        P(SHOT, SP),
        P(SHOT, None, None, SP, None),
        P(),
    )
    out_specs = P(SHOT + SP, None, None, None)
    return jax.shard_map(body, mesh=fine, in_specs=in_specs, out_specs=out_specs, check_vma=False)
```

```python
import jax
import jax.numpy as jnp
from jax import lax
from jax.sharding import Mesh, PartitionSpec as P

STEPS = 4
SHOT = ("x", "y", "zl")
SP = ("zh", "c")


def ring_gather(piece, axis):
    n = lax.psum(1, axis)
    me = lax.axis_index(axis)
    fwd = [(i, (i + 1) % n) for i in range(n)]
    bwd = [(i, (i - 1) % n) for i in range(n)]
    from_left = lax.ppermute(piece, axis, fwd)
    from_right = lax.ppermute(piece, axis, bwd)
    half = piece.shape[0] // 2
    far = jnp.concatenate(
        [lax.ppermute(from_left[:half], axis, fwd), lax.ppermute(from_right[half:], axis, bwd)], axis=0
    )
    rel = jnp.stack([piece, from_right, far, from_left], axis=0)
    doubled = jnp.concatenate([rel, rel], axis=0)
    return lax.dynamic_slice_in_dim(doubled, (n - me) % n, n, axis=0)


def gather_receivers(spectra, plan):
    n_shot = lax.psum(1, SHOT)
    sp_index = lax.axis_index(SP)
    shot_index = lax.axis_index(SHOT)
    column = lax.dynamic_index_in_dim(plan, sp_index, 1, keepdims=False)
    mine = column == shot_index
    owned_step = jnp.argmax(mine)
    block = lax.dynamic_index_in_dim(spectra, owned_step, 0, keepdims=False)
    parts, freq, kb, recv = block.shape
    split = n_shot // (parts * freq)
    pieces = block.reshape(parts * freq * split, kb // split, recv)
    got = lax.all_to_all(pieces, SHOT, 0, 0, tiled=True)
    chosen = jnp.take(got, column, axis=0)
    n_zl = lax.psum(1, "zl")
    me_zl = lax.axis_index("zl")
    other = lax.ppermute(chosen, "zl", [(i, n_zl - 1 - i) for i in range(n_zl)])
    pair = jnp.stack([chosen, other, chosen], axis=0)
    full = lax.dynamic_slice_in_dim(pair, (n_zl - me_zl) % n_zl, n_zl, axis=0)
    n_y, n_x, n_zl = lax.psum(1, "y"), lax.psum(1, "x"), full.shape[0]
    first = ring_gather(ring_gather(full[:, : STEPS // 2], "x"), "y")
    second = ring_gather(ring_gather(full[:, STEPS // 2 :], "y"), "x")
    full = jnp.concatenate([first, jnp.swapaxes(second, 0, 1)], axis=3)
    full = full.reshape(n_y, parts, n_x // parts, n_zl, STEPS, kb // split, recv)

    def part_of(p):
        return jnp.transpose(full[:, p], (1, 0, 3, 2, 4, 5)).reshape(freq, STEPS * kb, recv)

    return part_of(0), part_of(1)


def reduce_rows(out):
    n_zh = lax.psum(1, "zh")
    n_c = lax.psum(1, "c")
    zh = lax.axis_index("zh")
    c = lax.axis_index("c")
    rows = out.shape[0]
    blk = rows // (n_zh * n_c)
    x = out.reshape(n_zh, n_c, blk, *out.shape[1:])
    send = lax.dynamic_index_in_dim(x, n_c - 1 - c, 1, keepdims=False)
    keep = lax.dynamic_index_in_dim(x, c, 1, keepdims=False)
    got = lax.ppermute(send, "c", [(i, n_c - 1 - i) for i in range(n_c)])
    partial = keep + got
    half = blk // 2
    lo, hi = partial[:, :half], partial[:, half:]
    fwd = [(i, (i + 1) % n_zh) for i in range(n_zh)]
    bwd = [(i, (i - 1) % n_zh) for i in range(n_zh)]

    def chunk(a, index):
        return lax.dynamic_index_in_dim(a, index % n_zh, 0, keepdims=False)

    acc_lo = chunk(lo, zh + 2 * n_zh - 1)
    acc_hi = chunk(hi, zh + 1)
    for step in range(n_zh - 1):
        got_lo = lax.ppermute(acc_lo, "zh", fwd)
        got_hi = lax.ppermute(acc_hi, "zh", bwd)
        acc_lo = got_lo + chunk(lo, zh + 2 * n_zh - step - 2)
        acc_hi = got_hi + chunk(hi, zh + step + 2)
    return jnp.concatenate([acc_lo, acc_hi], axis=0)


def body(shot_data, live_masks, spectra, plan):
    live = shot_data * live_masks.astype(shot_data.dtype)[None, None]
    real_in, imag_in = gather_receivers(spectra, plan)
    freq, _, recv = real_in.shape
    weights = jnp.stack(
        [jnp.concatenate([real_in, imag_in], axis=-1), jnp.concatenate([-imag_in, real_in], axis=-1)], axis=0
    )
    half = freq // 2

    def product(lo, hi):
        out = lax.dot_general(
            live[:, lo:hi], weights[:, lo:hi], (((0, 3), (0, 2)), ((1,), (1,))), preferred_element_type=jnp.float32
        )
        return jnp.transpose(out, (1, 0, 2))

    by_scatter = lax.psum_scatter(product(0, half), SP, scatter_dimension=0, tiled=True)
    by_ring = reduce_rows(product(half, freq))
    out = jnp.concatenate([by_scatter, by_ring], axis=1)
    rows = out.shape[0]
    out = out.reshape(rows, freq, 2, recv).astype(jnp.bfloat16)
    return jnp.transpose(out, (0, 2, 1, 3))


def solution(mesh):
    n_shot = mesh.shape["shot"]
    n_sp = mesh.shape["sp"]
    devices = mesh.devices.reshape(n_shot // 8, 4, 2, n_sp // 2, 2)
    fine = Mesh(devices, ("x", "y", "zl", "zh", "c"))
    in_specs = (
        P(None, None, SHOT, SP),
        P(SHOT, SP),
        P(SHOT, None, None, SP, None),
        P(),
    )
    out_specs = P(SHOT + SP, None, None, None)
    return jax.shard_map(body, mesh=fine, in_specs=in_specs, out_specs=out_specs, check_vma=False)
```

```python
import jax
import jax.numpy as jnp
from jax import lax
from jax.sharding import Mesh, PartitionSpec as P

STEPS = 4
SHOT = ("x", "y", "zl")
SP = ("zh", "c")


def ring_gather(piece, axis):
    n = lax.psum(1, axis)
    me = lax.axis_index(axis)
    fwd = [(i, (i + 1) % n) for i in range(n)]
    bwd = [(i, (i - 1) % n) for i in range(n)]
    from_left = lax.ppermute(piece, axis, fwd)
    from_right = lax.ppermute(piece, axis, bwd)
    half = piece.shape[0] // 2
    far = jnp.concatenate(
        [lax.ppermute(from_left[:half], axis, fwd), lax.ppermute(from_right[half:], axis, bwd)], axis=0
    )
    rel = jnp.stack([piece, from_right, far, from_left], axis=0)
    doubled = jnp.concatenate([rel, rel], axis=0)
    return lax.dynamic_slice_in_dim(doubled, (n - me) % n, n, axis=0)


def gather_receivers(spectra, plan):
    n_shot = lax.psum(1, SHOT)
    sp_index = lax.axis_index(SP)
    shot_index = lax.axis_index(SHOT)
    column = lax.dynamic_index_in_dim(plan, sp_index, 1, keepdims=False)
    mine = column == shot_index
    owned_step = jnp.argmax(mine)
    block = lax.dynamic_index_in_dim(spectra, owned_step, 0, keepdims=False)
    parts, freq, kb, recv = block.shape
    split = n_shot // (parts * freq)
    pieces = block.reshape(parts * freq * split, kb // split, recv)
    got = lax.all_to_all(pieces, SHOT, 0, 0, tiled=True)
    chosen = jnp.take(got, column, axis=0)
    n_zl = lax.psum(1, "zl")
    me_zl = lax.axis_index("zl")
    other = lax.ppermute(chosen, "zl", [(i, n_zl - 1 - i) for i in range(n_zl)])
    pair = jnp.stack([chosen, other, chosen], axis=0)
    full = lax.dynamic_slice_in_dim(pair, (n_zl - me_zl) % n_zl, n_zl, axis=0)
    n_y, n_x, n_zl = lax.psum(1, "y"), lax.psum(1, "x"), full.shape[0]
    first = ring_gather(ring_gather(full[:, : STEPS // 2], "x"), "y")
    second = ring_gather(ring_gather(full[:, STEPS // 2 :], "y"), "x")
    full = jnp.concatenate([first, jnp.swapaxes(second, 0, 1)], axis=3)
    full = full.reshape(n_y, parts, n_x // parts, n_zl, STEPS, kb // split, recv)

    def part_of(p):
        return jnp.transpose(full[:, p], (1, 0, 3, 2, 4, 5)).reshape(freq, STEPS * kb, recv)

    return part_of(0), part_of(1)


def reduce_rows(out):
    n_zh = lax.psum(1, "zh")
    n_c = lax.psum(1, "c")
    zh = lax.axis_index("zh")
    c = lax.axis_index("c")
    rows = out.shape[0]
    blk = rows // (n_zh * n_c)
    x = out.reshape(n_zh, n_c, blk, *out.shape[1:])
    send = lax.dynamic_index_in_dim(x, n_c - 1 - c, 1, keepdims=False)
    keep = lax.dynamic_index_in_dim(x, c, 1, keepdims=False)
    got = lax.ppermute(send, "c", [(i, n_c - 1 - i) for i in range(n_c)])
    partial = keep + got
    half = blk // 2
    lo, hi = partial[:, :half], partial[:, half:]
    fwd = [(i, (i + 1) % n_zh) for i in range(n_zh)]
    bwd = [(i, (i - 1) % n_zh) for i in range(n_zh)]

    def chunk(a, index):
        return lax.dynamic_index_in_dim(a, index % n_zh, 0, keepdims=False)

    acc_lo = chunk(lo, zh + 2 * n_zh - 1)
    acc_hi = chunk(hi, zh + 1)
    for step in range(n_zh - 1):
        got_lo = lax.ppermute(acc_lo, "zh", fwd)
        got_hi = lax.ppermute(acc_hi, "zh", bwd)
        acc_lo = got_lo + chunk(lo, zh + 2 * n_zh - step - 2)
        acc_hi = got_hi + chunk(hi, zh + step + 2)
    return jnp.concatenate([acc_lo, acc_hi], axis=0)


def body(shot_data, live_masks, spectra, plan):
    live = shot_data * live_masks.astype(shot_data.dtype)[None, None]
    real_in, imag_in = gather_receivers(spectra, plan)
    freq, _, recv = real_in.shape
    weights = jnp.stack(
        [jnp.concatenate([real_in, imag_in], axis=-1), jnp.concatenate([-imag_in, real_in], axis=-1)], axis=0
    )
    half = (3 * freq) // 8

    def product(lo, hi):
        out = lax.dot_general(
            live[:, lo:hi], weights[:, lo:hi], (((0, 3), (0, 2)), ((1,), (1,))), preferred_element_type=jnp.float32
        )
        return jnp.transpose(out, (1, 0, 2))

    by_scatter = lax.psum_scatter(product(0, half), SP, scatter_dimension=0, tiled=True)
    by_ring = reduce_rows(product(half, freq))
    out = jnp.concatenate([by_scatter, by_ring], axis=1)
    rows = out.shape[0]
    out = out.reshape(rows, freq, 2, recv).astype(jnp.bfloat16)
    return jnp.transpose(out, (0, 2, 1, 3))


def solution(mesh):
    n_shot = mesh.shape["shot"]
    n_sp = mesh.shape["sp"]
    devices = mesh.devices.reshape(n_shot // 8, 4, 2, n_sp // 2, 2)
    fine = Mesh(devices, ("x", "y", "zl", "zh", "c"))
    in_specs = (
        P(None, None, SHOT, SP),
        P(SHOT, SP),
        P(SHOT, None, None, SP, None),
        P(),
    )
    out_specs = P(SHOT + SP, None, None, None)
    return jax.shard_map(body, mesh=fine, in_specs=in_specs, out_specs=out_specs, check_vma=False)
```

```python
import jax
import jax.numpy as jnp
from jax import lax
from jax.sharding import Mesh, PartitionSpec as P

STEPS = 4
SHOT = ("x", "y", "zl")
SP = ("zh", "c")


def ring_gather(piece, axis):
    n = lax.psum(1, axis)
    me = lax.axis_index(axis)
    fwd = [(i, (i + 1) % n) for i in range(n)]
    bwd = [(i, (i - 1) % n) for i in range(n)]
    from_left = lax.ppermute(piece, axis, fwd)
    from_right = lax.ppermute(piece, axis, bwd)
    half = piece.shape[0] // 2
    far = jnp.concatenate(
        [lax.ppermute(from_left[:half], axis, fwd), lax.ppermute(from_right[half:], axis, bwd)], axis=0
    )
    rel = jnp.stack([piece, from_right, far, from_left], axis=0)
    doubled = jnp.concatenate([rel, rel], axis=0)
    return lax.dynamic_slice_in_dim(doubled, (n - me) % n, n, axis=0)


def gather_receivers(spectra, plan):
    n_shot = lax.psum(1, SHOT)
    sp_index = lax.axis_index(SP)
    shot_index = lax.axis_index(SHOT)
    column = lax.dynamic_index_in_dim(plan, sp_index, 1, keepdims=False)
    mine = column == shot_index
    owned_step = jnp.argmax(mine)
    block = lax.dynamic_index_in_dim(spectra, owned_step, 0, keepdims=False)
    parts, freq, kb, recv = block.shape
    split = n_shot // (parts * freq)
    pieces = block.reshape(parts * freq * split, kb // split, recv)
    got = lax.all_to_all(pieces, SHOT, 0, 0, tiled=True)
    chosen = jnp.take(got, column, axis=0)
    n_zl = lax.psum(1, "zl")
    me_zl = lax.axis_index("zl")
    other = lax.ppermute(chosen, "zl", [(i, n_zl - 1 - i) for i in range(n_zl)])
    pair = jnp.stack([chosen, other, chosen], axis=0)
    full = lax.dynamic_slice_in_dim(pair, (n_zl - me_zl) % n_zl, n_zl, axis=0)
    n_y, n_x, n_zl = lax.psum(1, "y"), lax.psum(1, "x"), full.shape[0]
    first = ring_gather(ring_gather(full[:, : STEPS // 2], "x"), "y")
    second = ring_gather(ring_gather(full[:, STEPS // 2 :], "y"), "x")
    full = jnp.concatenate([first, jnp.swapaxes(second, 0, 1)], axis=3)
    full = full.reshape(n_y, parts, n_x // parts, n_zl, STEPS, kb // split, recv)

    def part_of(p):
        return jnp.transpose(full[:, p], (1, 0, 3, 2, 4, 5)).reshape(freq, STEPS * kb, recv)

    return part_of(0), part_of(1)


def reduce_rows(out):
    n_zh = lax.psum(1, "zh")
    n_c = lax.psum(1, "c")
    zh = lax.axis_index("zh")
    c = lax.axis_index("c")
    rows = out.shape[0]
    blk = rows // (n_zh * n_c)
    x = out.reshape(n_zh, n_c, blk, *out.shape[1:])
    send = lax.dynamic_index_in_dim(x, n_c - 1 - c, 1, keepdims=False)
    keep = lax.dynamic_index_in_dim(x, c, 1, keepdims=False)
    got = lax.ppermute(send, "c", [(i, n_c - 1 - i) for i in range(n_c)])
    partial = keep + got
    half = blk // 2
    lo, hi = partial[:, :half], partial[:, half:]
    fwd = [(i, (i + 1) % n_zh) for i in range(n_zh)]
    bwd = [(i, (i - 1) % n_zh) for i in range(n_zh)]

    def chunk(a, index):
        return lax.dynamic_index_in_dim(a, index % n_zh, 0, keepdims=False)

    acc_lo = chunk(lo, zh + 2 * n_zh - 1)
    acc_hi = chunk(hi, zh + 1)
    for step in range(n_zh - 1):
        got_lo = lax.ppermute(acc_lo, "zh", fwd)
        got_hi = lax.ppermute(acc_hi, "zh", bwd)
        acc_lo = got_lo + chunk(lo, zh + 2 * n_zh - step - 2)
        acc_hi = got_hi + chunk(hi, zh + step + 2)
    return jnp.concatenate([acc_lo, acc_hi], axis=0)


def body(shot_data, live_masks, spectra, plan):
    live = shot_data * live_masks.astype(shot_data.dtype)[None, None]
    real_in, imag_in = gather_receivers(spectra, plan)
    freq, _, recv = real_in.shape
    weights = jnp.stack(
        [jnp.concatenate([real_in, imag_in], axis=-1), jnp.concatenate([-imag_in, real_in], axis=-1)], axis=0
    )
    half = (5 * freq) // 8

    def product(lo, hi):
        out = lax.dot_general(
            live[:, lo:hi], weights[:, lo:hi], (((0, 3), (0, 2)), ((1,), (1,))), preferred_element_type=jnp.float32
        )
        return jnp.transpose(out, (1, 0, 2))

    by_scatter = lax.psum_scatter(product(0, half), SP, scatter_dimension=0, tiled=True)
    by_ring = reduce_rows(product(half, freq))
    out = jnp.concatenate([by_scatter, by_ring], axis=1)
    rows = out.shape[0]
    out = out.reshape(rows, freq, 2, recv).astype(jnp.bfloat16)
    return jnp.transpose(out, (0, 2, 1, 3))


def solution(mesh):
    n_shot = mesh.shape["shot"]
    n_sp = mesh.shape["sp"]
    devices = mesh.devices.reshape(n_shot // 8, 4, 2, n_sp // 2, 2)
    fine = Mesh(devices, ("x", "y", "zl", "zh", "c"))
    in_specs = (
        P(None, None, SHOT, SP),
        P(SHOT, SP),
        P(SHOT, None, None, SP, None),
        P(),
    )
    out_specs = P(SHOT + SP, None, None, None)
    return jax.shard_map(body, mesh=fine, in_specs=in_specs, out_specs=out_specs, check_vma=False)
```
